256 devices in a mesh: user: 16 (over y, z_hi, core), party: 16 (over x, z_lo).
Axes of the slice: x: 4, y: 4, z: 8 (z_hi: 2, z_lo: 4; z = z_hi * 4 + z_lo), core: 2. Of those that a mesh axis runs over, the one named last changes fastest.
Arguments:
- ratings: bfloat16 [1024, 16384], P('party', 'user'), may hold values from -6 to 6
- rating_mask: int32 [1024, 16384], P('party', 'user'), may hold values 0 or 1
- user_factors: bfloat16 [16384, 256], P('user'), may hold values from -0.375 to 0.375
- item_factors: bfloat16 [1024, 256], replicated, may hold values from -6 to 6
- item_index: int32 [1024], replicated, may hold values from 0 to 1023, each once
- features: bfloat16 [1024, 524288], P(None, ('user', 'party')), may hold values from -6 to 6
- ridge_weights: bfloat16 [524288, 256], P(('user', 'party')), may hold values from -10 to 10
Outputs:
- new_factors: float32 [1024, 256], P('party')
- fitted_weights: float32 [524288, 256], P(('user', 'party'))
The draws below stay inside these ranges and needn't reach their ends.
Inputs may be any that keep to these rules, and one draw needn't show every extreme that they name: `item_index`: each window item stands at exactly one tile position.
All inputs are finite; a program needn't handle non-finite values. No bound on the sum of `rating_mask` on one device may be relied on, other than what follows from the above.
Results may differ from the reference program's by a relative error of at most 0.00032.
Values may be sent and summed in bfloat16 or wider, within the bound.
No kernel may reach another device: no remote copies, remote signals or barrier semaphores. Data moves between devices by JAX's collectives and lax.ppermute only.
A program may use at most 64 MiB of HBM per device.

```python
import jax
import jax.numpy as jnp
from jax import lax

R = 256
F = 524288
ITERS = 2
ITEMS = 1024
USERS = 16384


def draw_ridge_weights(key, part):
    base_key, row_key, col_key = jax.random.split(jax.random.fold_in(key, 11), 3)
    position = jnp.arange(F, dtype=jnp.float32).reshape(F, 1) / float(F)
    base = jnp.clip(jax.random.normal(base_key, (F, R), jnp.float32), -3.5, 3.5)
    ramp = 1.15 * position
    row_scale = jnp.exp(ramp + jax.random.uniform(row_key, (F, 1), jnp.float32, -0.6, 0.6))
    col_scale = jnp.exp(jax.random.uniform(col_key, (1, R), jnp.float32, -0.6, 0.6))
    return (0.25 * base * row_scale * col_scale).astype(jnp.bfloat16)


def with_ends(entries, stream_key, low, high):
    spot = [jax.random.randint(jax.random.fold_in(stream_key, axis), (), 0, length) for axis, length in enumerate(entries.shape)]
    main_axis = entries.shape.index(max(entries.shape))
    beside = spot[:main_axis] + [(spot[main_axis] + 1) % entries.shape[main_axis]] + spot[main_axis + 1:]
    return entries.at[tuple(spot)].set(low).at[tuple(beside)].set(high)


def shard_levels(key, extent, shards, smallest, high):
    level = 1.0
    for axis_at, parts in shards:
        draws = jax.random.uniform(jax.random.fold_in(jax.random.fold_in(key, 6), axis_at), (parts,), jnp.float32, smallest / len(shards), high / len(shards))
        level = level * jnp.repeat(jnp.exp(draws), extent[axis_at] // parts).reshape((-1,) + (1,) * (len(extent) - 1 - axis_at))
    return level


def normal_values(stream_key, dims, spread, reach, cuts=(), kind=jnp.bfloat16):
    drawn = jax.random.normal(stream_key, dims, jnp.float32) * spread
    if len(cuts) > 0:
        drawn = shard_levels(stream_key, dims, cuts, -0.22, 0.18) * drawn
    return jnp.clip(drawn, min=-reach, max=reach).astype(kind)


def setup_inputs(seed: int = 0) -> dict:
    seeds = jax.random.split(jax.random.key(seed), 8)
    return {
        "ratings": normal_values(seeds[0], (ITEMS, USERS), 1.0, 6.0, ((0, 16), (1, 16))),
        "rating_mask": with_ends((jax.random.randint(seeds[1], (ITEMS, USERS), 0, 2) < 1).astype(jnp.int32), jax.random.fold_in(seeds[1], 1), 0, 1),
        "user_factors": normal_values(seeds[2], (USERS, R), R ** -0.5, 0.375, ((0, 16),)),
        "item_factors": normal_values(seeds[3], (ITEMS, R), 1.0, 6.0),
        "item_index": jax.random.permutation(seeds[4], ITEMS).astype(jnp.int32),
        "features": normal_values(seeds[5], (ITEMS, F), 1.0, 6.0, ((1, 256),)),
        "ridge_weights": draw_ridge_weights(jax.random.fold_in(seeds[7], 71), 0),
    }


learn_rate = 0.05
factor_decay = 1.0
ridge_decay = 0.05
ridge_step = 0.05

def reference(ratings, rating_mask, user_factors, item_factors, item_index, features, ridge_weights):
    tile_rows = item_factors[item_index.astype(jnp.int32)]
    scores = lax.dot_general(tile_rows, user_factors, (((1,), (1,)), ((), ())), preferred_element_type=jnp.float32)
    misfit = (rating_mask.astype(jnp.float32) * (scores - ratings.astype(jnp.float32))).astype(jnp.bfloat16)
    item_grad = jnp.dot(misfit, user_factors, preferred_element_type=jnp.float32)
    tile_wide = tile_rows.astype(jnp.float32)
    new_factors = tile_wide - learn_rate * (item_grad + factor_decay * tile_wide)
    targets = jnp.zeros((ITEMS, R), jnp.float32).at[item_index.astype(jnp.int32)].set(new_factors)
    feature_scale = 1.0 / math_sqrt(F)
    weights = ridge_weights.astype(jnp.float32)
    for iteration in range(ITERS):
        weights_bf = weights.astype(jnp.bfloat16)
        prediction = jnp.dot(features, weights_bf, preferred_element_type=jnp.float32) * feature_scale
        error_rows = (prediction - targets).astype(jnp.bfloat16)
        grad = lax.dot_general(features, error_rows, (((0,), (0,)), ((), ())), preferred_element_type=jnp.float32) * feature_scale + ridge_decay * weights
        mean_sq = jnp.mean(grad * grad)
        weights = weights - ridge_step * grad / jnp.sqrt(mean_sq + 1e-06)
    return (new_factors, weights)

def math_sqrt(value):
    return float(value) ** 0.5
```

```python
import jax
import jax.numpy as jnp
from jax import lax
from jax.sharding import PartitionSpec as P

ITERS = 2


learn_rate = 0.05
factor_decay = 1.0
ridge_decay = 0.05
ridge_step = 0.05

ALL = ("user", "party")


def reduce_scatter_rows(x, n):
    blocks = x.reshape(n, x.shape[0] // n, x.shape[1])
    return lax.all_to_all(blocks, ALL, 0, 0, tiled=True).sum(0)


def gather_rows(block, n):
    sent = jnp.broadcast_to(block[None], (n,) + block.shape)
    got = lax.all_to_all(sent, ALL, 0, 0, tiled=True)
    return got.reshape(n * block.shape[0], block.shape[1])


def sum_over_user(x):
    n = lax.axis_size("user")
    blocks = x.reshape(n, x.shape[0] // n, x.shape[1])
    block = lax.all_to_all(blocks, "user", 0, 0, tiled=True).sum(0)
    sent = jnp.broadcast_to(block[None], (n,) + block.shape)
    return lax.all_to_all(sent, "user", 0, 0, tiled=True).reshape(x.shape)


def total_scalar(value, n):
    sent = jnp.broadcast_to(value, (n, 1, 128))
    return lax.all_to_all(sent, ALL, 0, 0, tiled=True).sum(0)[0, 0]


def local(ratings, rating_mask, user_factors, item_factors, item_index, features, ridge_weights):
    local_items = ratings.shape[0]
    party_pos = lax.axis_index("party")
    user_pos = lax.axis_index("user")
    devices_all = lax.axis_size(ALL)
    local_index = lax.dynamic_slice_in_dim(item_index, party_pos * local_items, local_items)
    tile_rows = jnp.take(item_factors, local_index, axis=0)
    scores = lax.dot_general(
        tile_rows, user_factors, (((1,), (1,)), ((), ())), preferred_element_type=jnp.float32
    )
    misfit = (rating_mask.astype(jnp.float32) * (scores - ratings.astype(jnp.float32))).astype(
        jnp.bfloat16
    )
    partial_grad = jnp.dot(misfit, user_factors, preferred_element_type=jnp.float32)
    grad_total = sum_over_user(partial_grad)
    tile_wide = tile_rows.astype(jnp.float32)
    new_factors = tile_wide - learn_rate * (grad_total + factor_decay * tile_wide)
    own_tile = jnp.where(user_pos == 0, tile_wide - learn_rate * factor_decay * tile_wide, 0.0)
    share = learn_rate * partial_grad - own_tile
    items = item_factors.shape[0]
    minus_targets = jnp.zeros((items, share.shape[1]), jnp.float32).at[local_index].set(share)
    total_features = features.shape[1] * devices_all
    feature_scale = 1.0 / float(total_features) ** 0.5
    weights = ridge_weights.astype(jnp.float32)
    for iteration in range(ITERS):
        weights_bf = weights.astype(jnp.bfloat16)
        partial_pred = (
            jnp.dot(features, weights_bf, preferred_element_type=jnp.float32) * feature_scale
        )
        error_block = reduce_scatter_rows(partial_pred + minus_targets, devices_all)
        error_rows = gather_rows(error_block.astype(jnp.bfloat16), devices_all)
        grad = (
            lax.dot_general(
                features, error_rows, (((0,), (0,)), ((), ())), preferred_element_type=jnp.float32
            )
            * feature_scale
            + ridge_decay * weights
        )
        total_sq = total_scalar(jnp.sum(grad * grad), devices_all)
        mean_sq = total_sq / float(total_features * grad.shape[1])
        weights = weights - ridge_step * grad * lax.rsqrt(mean_sq + 1e-06)
    return (new_factors, weights)


def solution(mesh):
    in_specs = (
        P("party", "user"),
        P("party", "user"),
        P("user", None),
        P(),
        P(),
        P(None, ALL),
        P(ALL, None),
    )
    out_specs = (P("party", None), P(ALL, None))
    return jax.shard_map(local, mesh=mesh, in_specs=in_specs, out_specs=out_specs, check_vma=False)
```

```python
import jax
import jax.numpy as jnp
from jax import lax
from jax.sharding import PartitionSpec as P

ITERS = 2


learn_rate = 0.05
factor_decay = 1.0
ridge_decay = 0.05
ridge_step = 0.05

ALL = ("user", "party")


def reduce_scatter_rows(x, n):
    blocks = x.reshape(n, x.shape[0] // n, x.shape[1])
    return lax.all_to_all(blocks, ALL, 0, 0, tiled=True).sum(0)


def gather_rows(block, n):
    sent = jnp.broadcast_to(block[None], (n,) + block.shape)
    got = lax.all_to_all(sent, ALL, 0, 0, tiled=True)
    return got.reshape(n * block.shape[0], block.shape[1])


def sum_over_user(x):
    n = lax.axis_size("user")
    blocks = x.reshape(n, x.shape[0] // n, x.shape[1])
    block = lax.all_to_all(blocks, "user", 0, 0, tiled=True).sum(0)
    sent = jnp.broadcast_to(block[None], (n,) + block.shape)
    return lax.all_to_all(sent, "user", 0, 0, tiled=True).reshape(x.shape)


def total_scalar(value, n):
    sent = jnp.broadcast_to(value, (n, 1, 128))
    return lax.all_to_all(sent, ALL, 0, 0, tiled=True).sum(0)[0, 0]


def local(ratings, rating_mask, user_factors, item_factors, item_index, features, ridge_weights):
    local_items = ratings.shape[0]
    party_pos = lax.axis_index("party")
    user_pos = lax.axis_index("user")
    devices_all = lax.axis_size(ALL)
    local_index = lax.dynamic_slice_in_dim(item_index, party_pos * local_items, local_items)
    tile_rows = jnp.take(item_factors, local_index, axis=0)
    scores = lax.dot_general(
        tile_rows, user_factors, (((1,), (1,)), ((), ())), preferred_element_type=jnp.float32
    )
    misfit = (rating_mask.astype(jnp.float32) * (scores - ratings.astype(jnp.float32))).astype(
        jnp.bfloat16
    )
    partial_grad = jnp.dot(misfit, user_factors, preferred_element_type=jnp.float32)
    grad_total = sum_over_user(partial_grad)
    tile_wide = tile_rows.astype(jnp.float32)
    new_factors = tile_wide - learn_rate * (grad_total + factor_decay * tile_wide)
    share = jnp.where(user_pos == 0, -new_factors, 0.0)
    items = item_factors.shape[0]
    minus_targets = jnp.zeros((items, share.shape[1]), jnp.float32).at[local_index].set(share)
    total_features = features.shape[1] * devices_all
    feature_scale = 1.0 / float(total_features) ** 0.5
    weights = ridge_weights.astype(jnp.float32)
    for iteration in range(ITERS):
        weights_bf = weights.astype(jnp.bfloat16)
        partial_pred = (
            jnp.dot(features, weights_bf, preferred_element_type=jnp.float32) * feature_scale
        )
        error_block = reduce_scatter_rows(partial_pred + minus_targets, devices_all)
        error_rows = gather_rows(error_block.astype(jnp.bfloat16), devices_all)
        grad = (
            lax.dot_general(
                features, error_rows, (((0,), (0,)), ((), ())), preferred_element_type=jnp.float32
            )
            * feature_scale
            + ridge_decay * weights
        )
        total_sq = total_scalar(jnp.sum(grad * grad), devices_all)
        mean_sq = total_sq / float(total_features * grad.shape[1])
        weights = weights - ridge_step * grad * lax.rsqrt(mean_sq + 1e-06)
    return (new_factors, weights)


def solution(mesh):
    in_specs = (
        P("party", "user"),
        P("party", "user"),
        P("user", None),
        P(),
        P(),
        P(None, ALL),
        P(ALL, None),
    )
    out_specs = (P("party", None), P(ALL, None))
    return jax.shard_map(local, mesh=mesh, in_specs=in_specs, out_specs=out_specs, check_vma=False)
```

```python
import jax
import jax.numpy as jnp
from jax import lax
from jax.sharding import PartitionSpec as P

ITERS = 2


learn_rate = 0.05
factor_decay = 1.0
ridge_decay = 0.05
ridge_step = 0.05

ALL = ("user", "party")


def reduce_scatter_rows(x, n):
    blocks = x.reshape(n, x.shape[0] // n, x.shape[1])
    return lax.all_to_all(blocks, ALL, 0, 0, tiled=True).sum(0)


def gather_rows(block, n):
    sent = jnp.broadcast_to(block[None], (n,) + block.shape)
    got = lax.all_to_all(sent, ALL, 0, 0, tiled=True)
    return got.reshape(n * block.shape[0], block.shape[1])


def total_scalar(value, n):
    sent = jnp.broadcast_to(value, (n, 1, 128))
    return lax.all_to_all(sent, ALL, 0, 0, tiled=True).sum(0)[0, 0]


def body(ratings, rating_mask, user_factors, item_factors, item_index, features, ridge_weights):
    local_items = ratings.shape[0]
    party_pos = lax.axis_index("party")
    user_pos = lax.axis_index("user")
    devices_all = lax.axis_size(ALL)
    local_index = lax.dynamic_slice_in_dim(item_index, party_pos * local_items, local_items)
    tile_rows = jnp.take(item_factors, local_index, axis=0)
    scores = lax.dot_general(
        tile_rows, user_factors, (((1,), (1,)), ((), ())), preferred_element_type=jnp.float32
    )
    misfit = (rating_mask.astype(jnp.float32) * (scores - ratings.astype(jnp.float32))).astype(
        jnp.bfloat16
    )
    partial_grad = jnp.dot(misfit, user_factors, preferred_element_type=jnp.float32)
    grad_total = lax.psum(partial_grad, "user")
    tile_wide = tile_rows.astype(jnp.float32)
    new_factors = tile_wide - learn_rate * (grad_total + factor_decay * tile_wide)
    own_tile = jnp.where(user_pos == 0, tile_wide - learn_rate * factor_decay * tile_wide, 0.0)
    share = learn_rate * partial_grad - own_tile
    items = item_factors.shape[0]
    minus_targets = jnp.zeros((items, share.shape[1]), jnp.float32).at[local_index].set(share)
    total_features = features.shape[1] * devices_all
    feature_scale = 1.0 / float(total_features) ** 0.5
    weights = ridge_weights.astype(jnp.float32)
    for _ in range(ITERS):
        weights_bf = weights.astype(jnp.bfloat16)
        partial_pred = (
            jnp.dot(features, weights_bf, preferred_element_type=jnp.float32) * feature_scale
        )
        error_block = reduce_scatter_rows(partial_pred + minus_targets, devices_all)
        error_rows = gather_rows(error_block.astype(jnp.bfloat16), devices_all)
        grad = (
            lax.dot_general(
                features, error_rows, (((0,), (0,)), ((), ())), preferred_element_type=jnp.float32
            )
            * feature_scale
            + ridge_decay * weights
        )
        total_sq = total_scalar(jnp.sum(grad * grad), devices_all)
        mean_sq = total_sq / float(total_features * grad.shape[1])
        weights = weights - ridge_step * grad * lax.rsqrt(mean_sq + 1e-06)
    return (new_factors, weights)


def solution(mesh):
    in_specs = (
        P("party", "user"),
        P("party", "user"),
        P("user", None),
        P(),
        P(),
        P(None, ALL),
        P(ALL, None),
    )
    out_specs = (P("party", None), P(ALL, None))
    return jax.shard_map(body, mesh=mesh, in_specs=in_specs, out_specs=out_specs, check_vma=False)
```

```python
import jax
import jax.numpy as jnp
from jax import lax
from jax.sharding import PartitionSpec as P

ITERS = 2


learn_rate = 0.05
factor_decay = 1.0
ridge_decay = 0.05
ridge_step = 0.05

ALL = ("user", "party")


def reduce_scatter_tiles(x, n):
    rows, cols = x.shape
    tiles = x.reshape(rows // 8, 8, cols // 128, 128).transpose(0, 2, 1, 3).reshape(n, 8, 128)
    return lax.all_to_all(tiles, ALL, 0, 0, tiled=True).sum(0)


def gather_tiles(block, n, shape):
    rows, cols = shape
    sent = jnp.broadcast_to(block[None], (n,) + block.shape)
    got = lax.all_to_all(sent, ALL, 0, 0, tiled=True)
    return got.reshape(rows // 8, cols // 128, 8, 128).transpose(0, 2, 1, 3).reshape(rows, cols)


def total_scalar(value, n):
    sent = jnp.broadcast_to(value, (n, 1, 128))
    return lax.all_to_all(sent, ALL, 0, 0, tiled=True).sum(0)[0, 0]


def body(ratings, rating_mask, user_factors, item_factors, item_index, features, ridge_weights):
    local_items = ratings.shape[0]
    party_pos = lax.axis_index("party")
    user_pos = lax.axis_index("user")
    devices_all = lax.axis_size(ALL)
    local_index = lax.dynamic_slice_in_dim(item_index, party_pos * local_items, local_items)
    tile_rows = jnp.take(item_factors, local_index, axis=0)
    scores = lax.dot_general(
        tile_rows, user_factors, (((1,), (1,)), ((), ())), preferred_element_type=jnp.float32
    )
    misfit = (rating_mask.astype(jnp.float32) * (scores - ratings.astype(jnp.float32))).astype(
        jnp.bfloat16
    )
    partial_grad = jnp.dot(misfit, user_factors, preferred_element_type=jnp.float32)
    grad_total = lax.psum(partial_grad, "user")
    tile_wide = tile_rows.astype(jnp.float32)
    new_factors = tile_wide - learn_rate * (grad_total + factor_decay * tile_wide)
    own_tile = jnp.where(user_pos == 0, tile_wide - learn_rate * factor_decay * tile_wide, 0.0)
    share = learn_rate * partial_grad - own_tile
    items = item_factors.shape[0]
    minus_targets = jnp.zeros((items, share.shape[1]), jnp.float32).at[local_index].set(share)
    total_features = features.shape[1] * devices_all
    feature_scale = 1.0 / float(total_features) ** 0.5
    weights = ridge_weights.astype(jnp.float32)
    for _ in range(ITERS):
        weights_bf = weights.astype(jnp.bfloat16)
        partial_pred = (
            jnp.dot(features, weights_bf, preferred_element_type=jnp.float32) * feature_scale
        )
        error_block = reduce_scatter_tiles(partial_pred + minus_targets, devices_all)
        error_rows = gather_tiles(error_block.astype(jnp.bfloat16), devices_all, partial_pred.shape)
        grad = (
            lax.dot_general(
                features, error_rows, (((0,), (0,)), ((), ())), preferred_element_type=jnp.float32
            )
            * feature_scale
            + ridge_decay * weights
        )
        total_sq = total_scalar(jnp.sum(grad * grad), devices_all)
        mean_sq = total_sq / float(total_features * grad.shape[1])
        weights = weights - ridge_step * grad * lax.rsqrt(mean_sq + 1e-06)
    return (new_factors, weights)


def solution(mesh):
    in_specs = (
        P("party", "user"),
        P("party", "user"),
        P("user", None),
        P(),
        P(),
        P(None, ALL),
        P(ALL, None),
    )
    out_specs = (P("party", None), P(ALL, None))
    return jax.shard_map(body, mesh=mesh, in_specs=in_specs, out_specs=out_specs, check_vma=False)
```

```python
import jax
import jax.numpy as jnp
from jax import lax
from jax.sharding import PartitionSpec as P

ITERS = 2


learn_rate = 0.05
factor_decay = 1.0
ridge_decay = 0.05
ridge_step = 0.05

ALL = ("user", "party")


def reduce_scatter_tiles(x, n):
    rows, cols = x.shape
    tiles = x.reshape(rows // 8, 8, cols // 128, 128).transpose(0, 2, 1, 3).reshape(n, 8, 128)
    return lax.all_to_all(tiles, ALL, 0, 0, tiled=True).sum(0)


def gather_tiles(block, n, shape):
    rows, cols = shape
    sent = jnp.broadcast_to(block[None], (n,) + block.shape)
    got = lax.all_to_all(sent, ALL, 0, 0, tiled=True)
    return got.reshape(rows // 8, cols // 128, 8, 128).transpose(0, 2, 1, 3).reshape(rows, cols)


def sum_over_user(x):
    n = lax.axis_size("user")
    me = lax.axis_index("user")
    blocks = x.reshape(n, x.shape[0] // n, x.shape[1])
    order = (me - jnp.arange(n)) % n
    got = [lax.dynamic_index_in_dim(blocks, me, 0, keepdims=False)]
    for shift in range(1, n):
        sent = lax.dynamic_index_in_dim(blocks, (me + shift) % n, 0, keepdims=False)
        got.append(lax.ppermute(sent, "user", [(i, (i + shift) % n) for i in range(n)]))
    block = sum(got[1:], got[0])
    got = [block[None]]
    for shift in range(1, n):
        got.append(lax.ppermute(block, "user", [(i, (i + shift) % n) for i in range(n)])[None])
    return jnp.take(jnp.concatenate(got), order, axis=0).reshape(x.shape)


def total_scalar(value, n):
    sent = jnp.broadcast_to(value, (n, 1, 128))
    return lax.all_to_all(sent, ALL, 0, 0, tiled=True).sum(0)[0, 0]


def body(ratings, rating_mask, user_factors, item_factors, item_index, features, ridge_weights):
    local_items = ratings.shape[0]
    party_pos = lax.axis_index("party")
    user_pos = lax.axis_index("user")
    devices_all = lax.axis_size(ALL)
    local_index = lax.dynamic_slice_in_dim(item_index, party_pos * local_items, local_items)
    tile_rows = jnp.take(item_factors, local_index, axis=0)
    scores = lax.dot_general(
        tile_rows, user_factors, (((1,), (1,)), ((), ())), preferred_element_type=jnp.float32
    )
    misfit = (rating_mask.astype(jnp.float32) * (scores - ratings.astype(jnp.float32))).astype(
        jnp.bfloat16
    )
    partial_grad = jnp.dot(misfit, user_factors, preferred_element_type=jnp.float32)
    grad_total = sum_over_user(partial_grad)
    tile_wide = tile_rows.astype(jnp.float32)
    new_factors = tile_wide - learn_rate * (grad_total + factor_decay * tile_wide)
    own_tile = jnp.where(user_pos == 0, tile_wide - learn_rate * factor_decay * tile_wide, 0.0)
    share = learn_rate * partial_grad - own_tile
    items = item_factors.shape[0]
    minus_targets = jnp.zeros((items, share.shape[1]), jnp.float32).at[local_index].set(share)
    total_features = features.shape[1] * devices_all
    feature_scale = 1.0 / float(total_features) ** 0.5
    weights = ridge_weights.astype(jnp.float32)
    for _ in range(ITERS):
        weights_bf = weights.astype(jnp.bfloat16)
        partial_pred = (
            jnp.dot(features, weights_bf, preferred_element_type=jnp.float32) * feature_scale
        )
        error_block = reduce_scatter_tiles(partial_pred + minus_targets, devices_all)
        error_rows = gather_tiles(error_block.astype(jnp.bfloat16), devices_all, partial_pred.shape)
        grad = (
            lax.dot_general(
                features, error_rows, (((0,), (0,)), ((), ())), preferred_element_type=jnp.float32
            )
            * feature_scale
            + ridge_decay * weights
        )
        total_sq = total_scalar(jnp.sum(grad * grad), devices_all)
        mean_sq = total_sq / float(total_features * grad.shape[1])
        weights = weights - ridge_step * grad * lax.rsqrt(mean_sq + 1e-06)
    return (new_factors, weights)


def solution(mesh):
    in_specs = (
        P("party", "user"),
        P("party", "user"),
        P("user", None),
        P(),
        P(),
        P(None, ALL),
        P(ALL, None),
    )
    out_specs = (P("party", None), P(ALL, None))
    return jax.shard_map(body, mesh=mesh, in_specs=in_specs, out_specs=out_specs, check_vma=False)
```

```python
import jax
import jax.numpy as jnp
from jax import lax
from jax.experimental import pallas as pl
from jax.experimental.pallas import tpu as pltpu
from jax.sharding import PartitionSpec as P

ITERS = 2


learn_rate = 0.05
factor_decay = 1.0
ridge_decay = 0.05
ridge_step = 0.05

ALL = ("user", "party")


def reduce_scatter_tiles(x, n):
    rows, cols = x.shape
    tiles = x.reshape(rows // 8, 8, cols // 128, 128).transpose(0, 2, 1, 3).reshape(n, 8, 128)
    return lax.all_to_all(tiles, ALL, 0, 0, tiled=True).sum(0)


def gather_tiles(block, n, shape):
    rows, cols = shape
    sent = jnp.broadcast_to(block[None], (n,) + block.shape)
    got = lax.all_to_all(sent, ALL, 0, 0, tiled=True)
    return got.reshape(rows // 8, cols // 128, 8, 128).transpose(0, 2, 1, 3).reshape(rows, cols)


def total_scalar(value, n):
    sent = jnp.broadcast_to(value, (n, 1, 128))
    return lax.all_to_all(sent, ALL, 0, 0, tiled=True).sum(0)[0, 0]


def final_kernel(scale_ref, w_ref, *refs):
    *grad_refs, out_ref = refs
    w = w_ref[...].astype(jnp.float32)
    for k, grad_ref in enumerate(grad_refs):
        w = w - ridge_step * grad_ref[...].T * scale_ref[k]
    out_ref[...] = w


def final_weights(ridge_weights, grads, scales, block=1024):
    rows, cols = ridge_weights.shape
    grad_spec = pl.BlockSpec((cols, block), lambda i: (0, i))
    row_spec = pl.BlockSpec((block, cols), lambda i: (i, 0))
    return pl.pallas_call(
        final_kernel,
        grid=(rows // block,),
        in_specs=[pl.BlockSpec(memory_space=pltpu.SMEM), row_spec] + [grad_spec] * len(grads),
        out_specs=row_spec,
        out_shape=jax.ShapeDtypeStruct((rows, cols), jnp.float32),
    )(jnp.stack(scales), ridge_weights, *[g.T for g in grads])


def body(ratings, rating_mask, user_factors, item_factors, item_index, features, ridge_weights):
    local_items = ratings.shape[0]
    party_pos = lax.axis_index("party")
    user_pos = lax.axis_index("user")
    devices_all = lax.axis_size(ALL)
    local_index = lax.dynamic_slice_in_dim(item_index, party_pos * local_items, local_items)
    tile_rows = jnp.take(item_factors, local_index, axis=0)
    scores = lax.dot_general(
        tile_rows, user_factors, (((1,), (1,)), ((), ())), preferred_element_type=jnp.float32
    )
    misfit = (rating_mask.astype(jnp.float32) * (scores - ratings.astype(jnp.float32))).astype(
        jnp.bfloat16
    )
    partial_grad = jnp.dot(misfit, user_factors, preferred_element_type=jnp.float32)
    grad_total = lax.psum(partial_grad, "user")
    tile_wide = tile_rows.astype(jnp.float32)
    new_factors = tile_wide - learn_rate * (grad_total + factor_decay * tile_wide)
    own_tile = jnp.where(user_pos == 0, tile_wide - learn_rate * factor_decay * tile_wide, 0.0)
    share = learn_rate * partial_grad - own_tile
    items = item_factors.shape[0]
    minus_targets = jnp.zeros((items, share.shape[1]), jnp.float32).at[local_index].set(share)
    total_features = features.shape[1] * devices_all
    feature_scale = 1.0 / float(total_features) ** 0.5
    weights = ridge_weights.astype(jnp.float32)
    grads, scales = [], []
    for iteration in range(ITERS):
        weights_bf = weights.astype(jnp.bfloat16)
        partial_pred = (
            jnp.dot(features, weights_bf, preferred_element_type=jnp.float32) * feature_scale
        )
        error_block = reduce_scatter_tiles(partial_pred + minus_targets, devices_all)
        error_rows = gather_tiles(error_block.astype(jnp.bfloat16), devices_all, partial_pred.shape)
        grad = (
            lax.dot_general(
                features, error_rows, (((0,), (0,)), ((), ())), preferred_element_type=jnp.float32
            )
            * feature_scale
            + ridge_decay * weights
        )
        total_sq = total_scalar(jnp.sum(grad * grad), devices_all)
        mean_sq = total_sq / float(total_features * grad.shape[1])
        scale = lax.rsqrt(mean_sq + 1e-06)
        grads.append(grad)
        scales.append(scale)
        if iteration < ITERS - 1:
            weights = weights - ridge_step * grad * scale
    return (new_factors, final_weights(ridge_weights, grads, scales))


def solution(mesh):
    in_specs = (
        P("party", "user"),
        P("party", "user"),
        P("user", None),
        P(),
        P(),
        P(None, ALL),
        P(ALL, None),
    )
    out_specs = (P("party", None), P(ALL, None))
    return jax.shard_map(body, mesh=mesh, in_specs=in_specs, out_specs=out_specs, check_vma=False)
```

```python
import jax
import jax.numpy as jnp
from jax import lax
from jax.experimental import pallas as pl
from jax.experimental.pallas import tpu as pltpu
from jax.sharding import PartitionSpec as P

ITERS = 2


learn_rate = 0.05
factor_decay = 1.0
ridge_decay = 0.05
ridge_step = 0.05

ALL = ("user", "party")


def reduce_scatter_tiles(x, n):
    rows, cols = x.shape
    tiles = x.reshape(rows // 8, 8, cols // 128, 128).transpose(0, 2, 1, 3).reshape(n, 8, 128)
    return lax.all_to_all(tiles, ALL, 0, 0, tiled=True).sum(0)


def gather_tiles(block, n, shape):
    rows, cols = shape
    sent = jnp.broadcast_to(block[None], (n,) + block.shape)
    got = lax.all_to_all(sent, ALL, 0, 0, tiled=True)
    return got.reshape(rows // 8, cols // 128, 8, 128).transpose(0, 2, 1, 3).reshape(rows, cols)


def total_scalar(value, n):
    sent = jnp.broadcast_to(value, (n, 1, 128))
    return lax.all_to_all(sent, ALL, 0, 0, tiled=True).sum(0)[0, 0]


def ahead_kernel(scale_ref, w_ref, first_ref, last_ref, w_out_ref, last_out_ref):
    w = w_ref[...].astype(jnp.float32)
    w_out_ref[...] = w - ridge_step * first_ref[...].T * scale_ref[0]
    last_out_ref[...] = last_ref[...].T


def step_ahead(ridge_weights, first, scale, last, block=1024):
    rows, cols = ridge_weights.shape
    grad_spec = pl.BlockSpec((cols, block), lambda i: (0, i))
    row_spec = pl.BlockSpec((block, cols), lambda i: (i, 0))
    shape = jax.ShapeDtypeStruct((rows, cols), jnp.float32)
    return pl.pallas_call(
        ahead_kernel,
        grid=(rows // block,),
        in_specs=[pl.BlockSpec(memory_space=pltpu.SMEM), row_spec, grad_spec, grad_spec],
        out_specs=[row_spec, row_spec],
        out_shape=[shape, shape],
    )(scale.reshape(1), ridge_weights, first.T, last.T)


def body(ratings, rating_mask, user_factors, item_factors, item_index, features, ridge_weights):
    local_items = ratings.shape[0]
    party_pos = lax.axis_index("party")
    user_pos = lax.axis_index("user")
    devices_all = lax.axis_size(ALL)
    local_index = lax.dynamic_slice_in_dim(item_index, party_pos * local_items, local_items)
    tile_rows = jnp.take(item_factors, local_index, axis=0)
    scores = lax.dot_general(
        tile_rows, user_factors, (((1,), (1,)), ((), ())), preferred_element_type=jnp.float32
    )
    misfit = (rating_mask.astype(jnp.float32) * (scores - ratings.astype(jnp.float32))).astype(
        jnp.bfloat16
    )
    partial_grad = jnp.dot(misfit, user_factors, preferred_element_type=jnp.float32)
    grad_total = lax.psum(partial_grad, "user")
    tile_wide = tile_rows.astype(jnp.float32)
    new_factors = tile_wide - learn_rate * (grad_total + factor_decay * tile_wide)
    own_tile = jnp.where(user_pos == 0, tile_wide - learn_rate * factor_decay * tile_wide, 0.0)
    share = learn_rate * partial_grad - own_tile
    items = item_factors.shape[0]
    minus_targets = jnp.zeros((items, share.shape[1]), jnp.float32).at[local_index].set(share)
    total_features = features.shape[1] * devices_all
    feature_scale = 1.0 / float(total_features) ** 0.5
    weights = ridge_weights.astype(jnp.float32)
    grads, scales = [], []
    for iteration in range(ITERS):
        weights_bf = weights.astype(jnp.bfloat16)
        partial_pred = (
            jnp.dot(features, weights_bf, preferred_element_type=jnp.float32) * feature_scale
        )
        error_block = reduce_scatter_tiles(partial_pred + minus_targets, devices_all)
        error_rows = gather_tiles(error_block.astype(jnp.bfloat16), devices_all, partial_pred.shape)
        grad = (
            lax.dot_general(
                features, error_rows, (((0,), (0,)), ((), ())), preferred_element_type=jnp.float32
            )
            * feature_scale
            + ridge_decay * weights
        )
        total_sq = total_scalar(jnp.sum(grad * grad), devices_all)
        mean_sq = total_sq / float(total_features * grad.shape[1])
        scale = lax.rsqrt(mean_sq + 1e-06)
        grads.append(grad)
        scales.append(scale)
        if iteration < ITERS - 1:
            weights = weights - ridge_step * grad * scale
    stepped, last = step_ahead(ridge_weights, grads[0], scales[0], grads[1])
    return (new_factors, stepped - ridge_step * last * scales[1])


def solution(mesh):
    in_specs = (
        P("party", "user"),
        P("party", "user"),
        P("user", None),
        P(),
        P(),
        P(None, ALL),
        P(ALL, None),
    )
    out_specs = (P("party", None), P(ALL, None))
    return jax.shard_map(body, mesh=mesh, in_specs=in_specs, out_specs=out_specs, check_vma=False)
```

```python
import jax
import jax.numpy as jnp
from jax import lax
from jax.experimental import pallas as pl
from jax.experimental.pallas import tpu as pltpu
from jax.sharding import Mesh, PartitionSpec as P

ITERS = 2


learn_rate = 0.05
factor_decay = 1.0
ridge_decay = 0.05
ridge_step = 0.05

USER = ("user_outer", "core")
ALL = USER + ("party",)
OTHERS = ("user_outer", "party")


def to_tiles(x, n):
    rows, cols = x.shape
    return x.reshape(rows // 8, 8, cols // 128, 128).transpose(0, 2, 1, 3).reshape(n, 8, 128)


def from_tiles(tiles, shape):
    rows, cols = shape
    return tiles.reshape(rows // 8, cols // 128, 8, 128).transpose(0, 2, 1, 3).reshape(rows, cols)


def swap_cores(x):
    return lax.ppermute(x, "core", [(0, 1), (1, 0)])


def reduce_scatter_tiles(x):
    core = lax.axis_index("core")
    halves = x.reshape(2, x.shape[0] // 2, x.shape[1])
    mine = lax.dynamic_index_in_dim(halves, core, 0, keepdims=False)
    other = lax.dynamic_index_in_dim(halves, 1 - core, 0, keepdims=False)
    half = mine + swap_cores(other)
    n = lax.axis_size(OTHERS)
    return lax.all_to_all(to_tiles(half, n), OTHERS, 0, 0, tiled=True).sum(0)


def gather_tiles(block, shape):
    core = lax.axis_index("core")
    n = lax.axis_size(OTHERS)
    sent = jnp.broadcast_to(block[None], (n,) + block.shape)
    half = from_tiles(lax.all_to_all(sent, OTHERS, 0, 0, tiled=True), (shape[0] // 2, shape[1]))
    other = swap_cores(half)
    low = jnp.where(core == 0, half, other)
    high = jnp.where(core == 0, other, half)
    return jnp.concatenate([low, high])


def total_scalar(value, n):
    sent = jnp.broadcast_to(value, (n, 1, 128))
    return lax.all_to_all(sent, ALL, 0, 0, tiled=True).sum(0)[0, 0]


def ahead_kernel(scale_ref, w_ref, first_ref, last_ref, w_out_ref, last_out_ref):
    w = w_ref[...].astype(jnp.float32)
    w_out_ref[...] = w - ridge_step * first_ref[...].T * scale_ref[0]
    last_out_ref[...] = last_ref[...].T


def step_ahead(ridge_weights, first, scale, last, block=1024):
    rows, cols = ridge_weights.shape
    grad_spec = pl.BlockSpec((cols, block), lambda i: (0, i))
    row_spec = pl.BlockSpec((block, cols), lambda i: (i, 0))
    shape = jax.ShapeDtypeStruct((rows, cols), jnp.float32)
    return pl.pallas_call(
        ahead_kernel,
        grid=(rows // block,),
        in_specs=[pl.BlockSpec(memory_space=pltpu.SMEM), row_spec, grad_spec, grad_spec],
        out_specs=[row_spec, row_spec],
        out_shape=[shape, shape],
    )(scale.reshape(1), ridge_weights, first.T, last.T)


def body(ratings, rating_mask, user_factors, item_factors, item_index, features, ridge_weights):
    local_items = ratings.shape[0]
    party_pos = lax.axis_index("party")
    user_pos = lax.axis_index(USER)
    devices_all = lax.axis_size(ALL)
    local_index = lax.dynamic_slice_in_dim(item_index, party_pos * local_items, local_items)
    tile_rows = jnp.take(item_factors, local_index, axis=0)
    scores = lax.dot_general(
        tile_rows, user_factors, (((1,), (1,)), ((), ())), preferred_element_type=jnp.float32
    )
    misfit = (rating_mask.astype(jnp.float32) * (scores - ratings.astype(jnp.float32))).astype(
        jnp.bfloat16
    )
    partial_grad = jnp.dot(misfit, user_factors, preferred_element_type=jnp.float32)
    grad_total = lax.psum(partial_grad, USER)
    tile_wide = tile_rows.astype(jnp.float32)
    new_factors = tile_wide - learn_rate * (grad_total + factor_decay * tile_wide)
    own_tile = jnp.where(user_pos == 0, tile_wide - learn_rate * factor_decay * tile_wide, 0.0)
    share = learn_rate * partial_grad - own_tile
    items = item_factors.shape[0]
    minus_targets = jnp.zeros((items, share.shape[1]), jnp.float32).at[local_index].set(share)
    total_features = features.shape[1] * devices_all
    feature_scale = 1.0 / float(total_features) ** 0.5
    weights = ridge_weights.astype(jnp.float32)
    grads, scales = [], []
    for iteration in range(ITERS):
        weights_bf = weights.astype(jnp.bfloat16)
        partial_pred = (
            jnp.dot(features, weights_bf, preferred_element_type=jnp.float32) * feature_scale
        )
        error_block = reduce_scatter_tiles(partial_pred + minus_targets)
        error_rows = gather_tiles(error_block.astype(jnp.bfloat16), partial_pred.shape)
        grad = (
            lax.dot_general(
                features, error_rows, (((0,), (0,)), ((), ())), preferred_element_type=jnp.float32
            )
            * feature_scale
            + ridge_decay * weights
        )
        total_sq = total_scalar(jnp.sum(grad * grad), devices_all)
        mean_sq = total_sq / float(total_features * grad.shape[1])
        scale = lax.rsqrt(mean_sq + 1e-06)
        grads.append(grad)
        scales.append(scale)
        if iteration < ITERS - 1:
            weights = weights - ridge_step * grad * scale
    stepped, last = step_ahead(ridge_weights, grads[0], scales[0], grads[1])
    return (new_factors, stepped - ridge_step * last * scales[1])


def solution(mesh):
    users = mesh.shape["user"]
    grid = mesh.devices.reshape(users // 2, 2, mesh.shape["party"])
    mesh = Mesh(grid, ("user_outer", "core", "party"))
    in_specs = (
        P("party", USER),
        P("party", USER),
        P(USER, None),
        P(),
        P(),
        P(None, ALL),
        P(ALL, None),
    )
    out_specs = (P("party", None), P(ALL, None))
    return jax.shard_map(body, mesh=mesh, in_specs=in_specs, out_specs=out_specs, check_vma=False)
```

```python
import jax
import jax.numpy as jnp
from jax import lax
from jax.experimental import pallas as pl
from jax.experimental.pallas import tpu as pltpu
from jax.sharding import Mesh, PartitionSpec as P

ITERS = 2


learn_rate = 0.05
factor_decay = 1.0
ridge_decay = 0.05
ridge_step = 0.05

USER = ("user_outer", "core")
PARTY = ("x_outer", "x_pair", "party_inner")
ALL = USER + PARTY
OTHERS = ("user_outer", "x_outer", "party_inner")


def to_tiles(x, n):
    rows, cols = x.shape
    return x.reshape(rows // 8, 8, cols // 128, 128).transpose(0, 2, 1, 3).reshape(n, 8, 128)


def from_tiles(tiles, shape):
    rows, cols = shape
    return tiles.reshape(rows // 8, cols // 128, 8, 128).transpose(0, 2, 1, 3).reshape(rows, cols)


def swap(x, axis):
    return lax.ppermute(x, axis, [(0, 1), (1, 0)])


def halve(x, axis):
    side = lax.axis_index(axis)
    halves = x.reshape(2, x.shape[0] // 2, x.shape[1])
    mine = lax.dynamic_index_in_dim(halves, side, 0, keepdims=False)
    other = lax.dynamic_index_in_dim(halves, 1 - side, 0, keepdims=False)
    return mine + swap(other, axis)


def double(x, axis):
    side = lax.axis_index(axis)
    other = swap(x, axis)
    low = jnp.where(side == 0, x, other)
    high = jnp.where(side == 0, other, x)
    return jnp.concatenate([low, high])


def reduce_scatter_tiles(x):
    part = halve(halve(x, "core"), "x_pair")
    n = lax.axis_size(OTHERS)
    return lax.all_to_all(to_tiles(part, n), OTHERS, 0, 0, tiled=True).sum(0)


def gather_tiles(block, shape):
    n = lax.axis_size(OTHERS)
    sent = jnp.broadcast_to(block[None], (n,) + block.shape)
    part = from_tiles(lax.all_to_all(sent, OTHERS, 0, 0, tiled=True), (shape[0] // 4, shape[1]))
    return double(double(part, "x_pair"), "core")


def total_scalar(value, n):
    sent = jnp.broadcast_to(value, (n, 1, 128))
    return lax.all_to_all(sent, ALL, 0, 0, tiled=True).sum(0)[0, 0]


def ahead_kernel(scale_ref, w_ref, first_ref, last_ref, w_out_ref, last_out_ref):
    w = w_ref[...].astype(jnp.float32)
    w_out_ref[...] = w - ridge_step * first_ref[...].T * scale_ref[0]
    last_out_ref[...] = last_ref[...].T


def step_ahead(ridge_weights, first, scale, last, block=1024):
    rows, cols = ridge_weights.shape
    grad_spec = pl.BlockSpec((cols, block), lambda i: (0, i))
    row_spec = pl.BlockSpec((block, cols), lambda i: (i, 0))
    shape = jax.ShapeDtypeStruct((rows, cols), jnp.float32)
    return pl.pallas_call(
        ahead_kernel,
        grid=(rows // block,),
        in_specs=[pl.BlockSpec(memory_space=pltpu.SMEM), row_spec, grad_spec, grad_spec],
        out_specs=[row_spec, row_spec],
        out_shape=[shape, shape],
    )(scale.reshape(1), ridge_weights, first.T, last.T)


def body(ratings, rating_mask, user_factors, item_factors, item_index, features, ridge_weights):
    local_items = ratings.shape[0]
    party_pos = lax.axis_index(PARTY)
    user_pos = lax.axis_index(USER)
    devices_all = lax.axis_size(ALL)
    local_index = lax.dynamic_slice_in_dim(item_index, party_pos * local_items, local_items)
    tile_rows = jnp.take(item_factors, local_index, axis=0)
    scores = lax.dot_general(
        tile_rows, user_factors, (((1,), (1,)), ((), ())), preferred_element_type=jnp.float32
    )
    misfit = (rating_mask.astype(jnp.float32) * (scores - ratings.astype(jnp.float32))).astype(
        jnp.bfloat16
    )
    partial_grad = jnp.dot(misfit, user_factors, preferred_element_type=jnp.float32)
    grad_total = lax.psum(partial_grad, USER)
    tile_wide = tile_rows.astype(jnp.float32)
    new_factors = tile_wide - learn_rate * (grad_total + factor_decay * tile_wide)
    own_tile = jnp.where(user_pos == 0, tile_wide - learn_rate * factor_decay * tile_wide, 0.0)
    share = learn_rate * partial_grad - own_tile
    items = item_factors.shape[0]
    minus_targets = jnp.zeros((items, share.shape[1]), jnp.float32).at[local_index].set(share)
    total_features = features.shape[1] * devices_all
    feature_scale = 1.0 / float(total_features) ** 0.5
    weights = ridge_weights.astype(jnp.float32)
    grads, scales = [], []
    for iteration in range(ITERS):
        weights_bf = weights.astype(jnp.bfloat16)
        partial_pred = (
            jnp.dot(features, weights_bf, preferred_element_type=jnp.float32) * feature_scale
        )
        error_block = reduce_scatter_tiles(partial_pred + minus_targets)
        error_rows = gather_tiles(error_block.astype(jnp.bfloat16), partial_pred.shape)
        grad = (
            lax.dot_general(
                features, error_rows, (((0,), (0,)), ((), ())), preferred_element_type=jnp.float32
            )
            * feature_scale
            + ridge_decay * weights
        )
        total_sq = total_scalar(jnp.sum(grad * grad), devices_all)
        mean_sq = total_sq / float(total_features * grad.shape[1])
        scale = lax.rsqrt(mean_sq + 1e-06)
        grads.append(grad)
        scales.append(scale)
        if iteration < ITERS - 1:
            weights = weights - ridge_step * grad * scale
    stepped, last = step_ahead(ridge_weights, grads[0], scales[0], grads[1])
    return (new_factors, stepped - ridge_step * last * scales[1])


def solution(mesh):
    users = mesh.shape["user"]
    parties = mesh.shape["party"]
    grid = mesh.devices.reshape(users // 2, 2, 2, 2, parties // 4)
    mesh = Mesh(grid, USER + PARTY)
    in_specs = (
        P(PARTY, USER),
        P(PARTY, USER),
        P(USER, None),
        P(),
        P(),
        P(None, ALL),
        P(ALL, None),
    )
    out_specs = (P(PARTY, None), P(ALL, None))
    return jax.shard_map(body, mesh=mesh, in_specs=in_specs, out_specs=out_specs, check_vma=False)
```

```python
import jax
import jax.numpy as jnp
from jax import lax
from jax.experimental import pallas as pl
from jax.experimental.pallas import tpu as pltpu
from jax.sharding import Mesh, PartitionSpec as P

ITERS = 2


learn_rate = 0.05
factor_decay = 1.0
ridge_decay = 0.05
ridge_step = 0.05

USER = ("user_outer", "core")
ALL = USER + ("party",)
OTHERS = ("user_outer", "party")


def to_tiles(x, n):
    rows, cols = x.shape
    return x.reshape(rows // 8, 8, cols // 128, 128).transpose(0, 2, 1, 3).reshape(n, 8, 128)


def from_tiles(tiles, shape):
    rows, cols = shape
    return tiles.reshape(rows // 8, cols // 128, 8, 128).transpose(0, 2, 1, 3).reshape(rows, cols)


def swap_cores(x):
    return lax.ppermute(x, "core", [(0, 1), (1, 0)])


def reduce_scatter_tiles(x):
    core = lax.axis_index("core")
    halves = x.reshape(2, x.shape[0] // 2, x.shape[1])
    mine = lax.dynamic_index_in_dim(halves, core, 0, keepdims=False)
    other = lax.dynamic_index_in_dim(halves, 1 - core, 0, keepdims=False)
    half = mine + swap_cores(other)
    n = lax.axis_size(OTHERS)
    return lax.all_to_all(to_tiles(half, n), OTHERS, 0, 0, tiled=True).sum(0)


def gather_tiles(block, shape):
    core = lax.axis_index("core")
    n = lax.axis_size(OTHERS)
    sent = jnp.broadcast_to(block[None], (n,) + block.shape)
    half = from_tiles(lax.all_to_all(sent, OTHERS, 0, 0, tiled=True), (shape[0] // 2, shape[1]))
    other = swap_cores(half)
    low = jnp.where(core == 0, half, other)
    high = jnp.where(core == 0, other, half)
    return jnp.concatenate([low, high])


def total_scalar(value, n):
    sent = jnp.broadcast_to(value, (n, 1, 128))
    return lax.all_to_all(sent, ALL, 0, 0, tiled=True).sum(0)[0, 0]


def ahead_kernel(scale_ref, w_ref, first_ref, last_ref, w_out_ref, last_out_ref):
    w = w_ref[...].astype(jnp.float32)
    w_out_ref[...] = w - ridge_step * first_ref[...].T * scale_ref[0]
    last_out_ref[...] = last_ref[...].T


def step_ahead(ridge_weights, first, scale, last, block=1024):
    rows, cols = ridge_weights.shape
    grad_spec = pl.BlockSpec((cols, block), lambda i: (0, i))
    row_spec = pl.BlockSpec((block, cols), lambda i: (i, 0))
    shape = jax.ShapeDtypeStruct((rows, cols), jnp.float32)
    return pl.pallas_call(
        ahead_kernel,
        grid=(rows // block,),
        in_specs=[pl.BlockSpec(memory_space=pltpu.SMEM), row_spec, grad_spec, grad_spec],
        out_specs=[row_spec, row_spec],
        out_shape=[shape, shape],
    )(scale.reshape(1), ridge_weights, first.T, last.T)


def body(ratings, rating_mask, user_factors, item_factors, item_index, features, ridge_weights):
    local_items = ratings.shape[0]
    party_pos = lax.axis_index("party")
    user_pos = lax.axis_index(USER)
    devices_all = lax.axis_size(ALL)
    local_index = lax.dynamic_slice_in_dim(item_index, party_pos * local_items, local_items)
    tile_rows = jnp.take(item_factors, local_index, axis=0)
    scores = lax.dot_general(
        tile_rows, user_factors, (((1,), (1,)), ((), ())), preferred_element_type=jnp.float32
    )
    misfit = (rating_mask.astype(jnp.float32) * (scores - ratings.astype(jnp.float32))).astype(
        jnp.bfloat16
    )
    partial_grad = jnp.dot(misfit, user_factors, preferred_element_type=jnp.float32)
    grad_total = lax.psum(partial_grad, USER)
    tile_wide = tile_rows.astype(jnp.float32)
    new_factors = tile_wide - learn_rate * (grad_total + factor_decay * tile_wide)
    own_tile = jnp.where(user_pos == 0, tile_wide - learn_rate * factor_decay * tile_wide, 0.0)
    share = learn_rate * partial_grad - own_tile
    items = item_factors.shape[0]
    minus_targets = jnp.zeros((items, share.shape[1]), jnp.float32).at[local_index].set(share)
    total_features = features.shape[1] * devices_all
    feature_scale = 1.0 / float(total_features) ** 0.5
    weights_t = lax.optimization_barrier(ridge_weights.T)
    weights = weights_t.T.astype(jnp.float32)
    grads, scales = [], []
    for iteration in range(ITERS):
        weights_bf = ridge_weights if iteration == 0 else weights.astype(jnp.bfloat16)
        partial_pred = (
            jnp.dot(features, weights_bf, preferred_element_type=jnp.float32) * feature_scale
        )
        error_block = reduce_scatter_tiles(partial_pred + minus_targets)
        error_rows = gather_tiles(error_block.astype(jnp.bfloat16), partial_pred.shape)
        grad = (
            lax.dot_general(
                features, error_rows, (((0,), (0,)), ((), ())), preferred_element_type=jnp.float32
            )
            * feature_scale
            + ridge_decay * weights
        )
        total_sq = total_scalar(jnp.sum(grad * grad), devices_all)
        mean_sq = total_sq / float(total_features * grad.shape[1])
        scale = lax.rsqrt(mean_sq + 1e-06)
        grads.append(grad)
        scales.append(scale)
        if iteration < ITERS - 1:
            weights = weights - ridge_step * grad * scale
    stepped, last = step_ahead(ridge_weights, grads[0], scales[0], grads[1])
    return (new_factors, stepped - ridge_step * last * scales[1])


def solution(mesh):
    users = mesh.shape["user"]
    grid = mesh.devices.reshape(users // 2, 2, mesh.shape["party"])
    mesh = Mesh(grid, ("user_outer", "core", "party"))
    in_specs = (
        P("party", USER),
        P("party", USER),
        P(USER, None),
        P(),
        P(),
        P(None, ALL),
        P(ALL, None),
    )
    out_specs = (P("party", None), P(ALL, None))
    return jax.shard_map(body, mesh=mesh, in_specs=in_specs, out_specs=out_specs, check_vma=False)
```
